512 devices in a mesh: op: 16 (over y_lo, z), bond: 32 (over y_hi, x, core).
Axes of the slice: x: 4, y: 8 (y_hi: 4, y_lo: 2; y = y_hi * 2 + y_lo), z: 8, core: 2. Of those that a mesh axis runs over, the one named last changes fastest.
Arguments:
- vectors: bfloat16 [2, 64, 256, 256], P(None, 'bond'), may hold values from -6 to 6
- left_ops: bfloat16 [128, 64, 256, 256], P('op', 'bond'), may hold values from -0.03125 to 0.03125
- right_ops: bfloat16 [128, 64, 256, 256], P('op', 'bond'), may hold values from -0.375 to 0.375
- block_sizes: int32 [64, 2], P('bond'), may hold values from 32 to 256, as said below
- term_shifts: int32 [128], P('op'), may hold values from -1 to 1
Outputs:
- sigma: float32 [2, 64, 256, 256], P(None, 'bond', 'op')
The draws below stay inside these ranges and needn't reach their ends.
Inputs may be any that keep to these rules, and one draw needn't show every extreme that they name: `block_sizes`: some block has both live dimensions 256 and some other block both 256 // 8.
All inputs are finite; a program needn't handle non-finite values.
Results may differ from the reference program's by a relative error of at most 0.0029.
Values may be sent and summed in bfloat16 or wider, within the bound.
No kernel may reach another device: no remote copies, remote signals or barrier semaphores. Data moves between devices by JAX's collectives and lax.ppermute only.
A program may use at most 64 MiB of HBM per device.

```python
import jax
import jax.numpy as jnp
from jax import lax

S = 256
NVEC = 2
NBLK = 64
NTERM = 128


def draw_block_sizes(key, part):
    key_sizes, key_full, key_offset = jax.random.split(key, 3)
    block_table = jax.random.randint(key_sizes, (NBLK, 2), S // 8, S + 1, dtype=jnp.int32)
    full_block = jax.random.randint(key_full, (), 0, NBLK, dtype=jnp.int32)
    offset = jax.random.randint(key_offset, (), 1, NBLK, dtype=jnp.int32)
    small_block = (full_block + offset) % NBLK
    block_table = block_table.at[full_block].set(S)
    block_table = block_table.at[small_block].set(S // 8)
    return block_table


def touch_ends(values, stream_key, smallest, top_value):
    index_at = [jax.random.randint(jax.random.fold_in(stream_key, axis), (), 0, length) for axis, length in enumerate(values.shape)]
    widest = values.shape.index(max(values.shape))
    beside = index_at[:widest] + [(index_at[widest] + 1) % values.shape[widest]] + index_at[widest + 1:]
    return values.at[tuple(index_at)].set(smallest).at[tuple(beside)].set(top_value)


def steps_of(rng, dims, shards, smallest, largest):
    factor_of, own = 1.0, jax.random.fold_in(rng, 6)
    for dim, shards_of in shards:
        steps = jnp.exp(jax.random.uniform(jax.random.fold_in(own, dim), (shards_of,), jnp.float32, smallest / len(shards), largest / len(shards)))
        factor_of = factor_of * jnp.repeat(steps, dims[dim] // shards_of).reshape([-1 if axis == dim else 1 for axis in range(len(dims))])
    return factor_of


def gaussian(key, shape, deviation, reach, shards=(), kind=jnp.bfloat16):
    factor_of = steps_of(key, shape, shards, -0.22, 0.18) if shards else 1.0
    values = jax.random.normal(key, shape, jnp.float32) * deviation * factor_of
    return jnp.minimum(jnp.maximum(values, -reach), reach).astype(kind)


def setup_inputs(seed: int = 0) -> dict:
    seeds = jax.random.split(jax.random.key(seed), 6)
    return {
        "vectors": gaussian(seeds[0], (NVEC, NBLK, S, S), 1.0, 6.0, ((1, 32),)),
        "left_ops": gaussian(seeds[1], (NTERM, NBLK, S, S), (S * NTERM) ** -0.5, 0.03125, ((0, 16), (1, 32))),
        "right_ops": gaussian(seeds[2], (NTERM, NBLK, S, S), S ** -0.5, 0.375, ((0, 16), (1, 32))),
        "block_sizes": draw_block_sizes(jax.random.fold_in(seeds[5], 71), 0),
        "term_shifts": touch_ends(jax.random.randint(seeds[4], (NTERM,), -1, 2), jax.random.fold_in(seeds[4], 1), -1, 1).astype(jnp.int32),
    }


def reference(vectors, left_ops, right_ops, block_sizes, term_shifts):
    row_index = jnp.arange(S, dtype=jnp.int32)
    live_mask = (row_index[None, :, None] < block_sizes[:, 0][:, None, None]) & (row_index[None, None, :] < block_sizes[:, 1][:, None, None])
    masked = jnp.where(live_mask[None], vectors, jnp.zeros((), vectors.dtype))
    padded = jnp.pad(masked, ((0, 0), (1, 1), (0, 0), (0, 0)))

    def add_term(accumulated, operands):
        left_block, right_block, term_shift = operands
        start_block = (1 - term_shift).astype(jnp.int32)
        source_blocks = lax.dynamic_slice_in_dim(padded, start_block, NBLK, 1)
        half_product = jnp.einsum('bik,vbkj->vbij', left_block.astype(jnp.float32), source_blocks.astype(jnp.float32)).astype(jnp.bfloat16)
        half_product = lax.optimization_barrier(half_product)
        term_value = jnp.einsum('vbij,blj->vbil', half_product.astype(jnp.float32), right_block.astype(jnp.float32))
        return accumulated + term_value, None

    initial = jnp.zeros((NVEC, NBLK, S, S), jnp.float32)
    accumulated, _ = lax.scan(add_term, initial, (left_ops, right_ops, term_shifts))
    return jnp.where(live_mask[None], accumulated, jnp.zeros((), accumulated.dtype))
```

```python
import jax
import jax.numpy as jnp
from jax import lax
from jax.sharding import PartitionSpec as P


def extended(cells, axis, dim):
    count = lax.axis_size(axis)
    ends = count - 1
    head = lax.slice_in_dim(cells, 0, 1, axis=dim)
    tail = lax.slice_in_dim(cells, cells.shape[dim] - 1, cells.shape[dim], axis=dim)
    return jnp.concatenate(
        [
            lax.ppermute(tail, axis, [(i, (i + 1) % count) for i in range(ends)]),
            cells,
            lax.ppermute(head, axis, [((i + 1) % count, i) for i in range(ends)]),
        ],
        axis=dim,
    )


def per_device(vectors, left_ops, right_ops, block_sizes, term_shifts):
    block_count = vectors.shape[1]
    block_order = vectors.shape[2]
    row_index = jnp.arange(block_order, dtype=jnp.int32)
    live_mask = (row_index[None, :, None] < block_sizes[:, 0][:, None, None]) & (
        row_index[None, None, :] < block_sizes[:, 1][:, None, None]
    )
    masked = jnp.where(live_mask[None], vectors, jnp.zeros((), vectors.dtype))
    padded = extended(masked, "bond", 1)

    shift = term_shifts[:, None, None, None, None]
    sources = jnp.where(
        shift == 1,
        padded[None, :, 0:block_count],
        jnp.where(shift == 0, padded[None, :, 1 : block_count + 1], padded[None, :, 2 : block_count + 2]),
    )
    half = jnp.einsum(
        "tbik,tvbkj->tvbij", left_ops, sources, preferred_element_type=jnp.float32
    ).astype(jnp.bfloat16)
    partial = jnp.einsum("tvbij,tblj->vbil", half, right_ops, preferred_element_type=jnp.float32)

    op_count = lax.axis_size("op")
    share_rows = block_order // op_count
    shares = partial.reshape(partial.shape[0], block_count, op_count, share_rows, block_order)
    received = lax.all_to_all(shares, "op", 2, 2, tiled=False)
    own_share = received.sum(axis=2)
    first_row = lax.axis_index("op") * share_rows
    live_share = lax.dynamic_slice_in_dim(live_mask, first_row, share_rows, 1)
    return jnp.where(live_share[None], own_share, jnp.zeros((), own_share.dtype))


def solution(mesh):
    in_specs = (
        P(None, "bond", None, None),
        P("op", "bond", None, None),
        P("op", "bond", None, None),
        P("bond", None),
        P("op"),
    )
    out_specs = P(None, "bond", "op", None)
    return jax.shard_map(
        per_device, mesh=mesh, in_specs=in_specs, out_specs=out_specs, check_vma=False
    )
```

```python
import jax
import jax.numpy as jnp
from jax import lax
from jax.sharding import PartitionSpec as P


def extended(cells, axis, dim):
    count = lax.axis_size(axis)
    ends = count - 1
    head = lax.slice_in_dim(cells, 0, 1, axis=dim)
    tail = lax.slice_in_dim(cells, cells.shape[dim] - 1, cells.shape[dim], axis=dim)
    return jnp.concatenate(
        [
            lax.ppermute(tail, axis, [(i, (i + 1) % count) for i in range(ends)]),
            cells,
            lax.ppermute(head, axis, [((i + 1) % count, i) for i in range(ends)]),
        ],
        axis=dim,
    )


def per_device(vectors, left_ops, right_ops, block_sizes, term_shifts):
    block_count = vectors.shape[1]
    block_order = vectors.shape[2]
    row_index = jnp.arange(block_order, dtype=jnp.int32)
    live_mask = (row_index[None, :, None] < block_sizes[:, 0][:, None, None]) & (
        row_index[None, None, :] < block_sizes[:, 1][:, None, None]
    )
    masked = jnp.where(live_mask[None], vectors, jnp.zeros((), vectors.dtype))
    padded = extended(masked, "bond", 1)

    shift = term_shifts[:, None, None, None, None]
    sources = jnp.where(
        shift == 1,
        padded[None, :, 0:block_count],
        jnp.where(shift == 0, padded[None, :, 1 : block_count + 1], padded[None, :, 2 : block_count + 2]),
    )
    op_count = lax.axis_size("op")
    share_rows = block_order // op_count
    half = jnp.einsum(
        "tbik,tvbkj->tvbij", left_ops, sources, preferred_element_type=jnp.float32
    ).astype(jnp.bfloat16)
    partial = jnp.einsum("tvbij,tblj->vbil", half, right_ops, preferred_element_type=jnp.float32)

    shares = partial.astype(jnp.bfloat16).reshape(
        partial.shape[0], block_count, op_count, share_rows, block_order
    )
    received = lax.all_to_all(shares, "op", 2, 2, tiled=False)
    own_share = received.astype(jnp.float32).sum(axis=2)
    first_row = lax.axis_index("op") * share_rows
    live_share = lax.dynamic_slice_in_dim(live_mask, first_row, share_rows, 1)
    return jnp.where(live_share[None], own_share, jnp.zeros((), own_share.dtype))


def solution(mesh):
    in_specs = (
        P(None, "bond", None, None),
        P("op", "bond", None, None),
        P("op", "bond", None, None),
        P("bond", None),
        P("op"),
    )
    out_specs = P(None, "bond", "op", None)
    return jax.shard_map(
        per_device, mesh=mesh, in_specs=in_specs, out_specs=out_specs, check_vma=False
    )
```

```python
import jax
import jax.numpy as jnp
from jax import lax
from jax.sharding import PartitionSpec as P


def per_device(vectors, left_ops, right_ops, block_sizes, term_shifts):
    block_order = vectors.shape[2]
    row_index = jnp.arange(block_order, dtype=jnp.int32)
    live_mask = (row_index[None, :, None] < block_sizes[:, 0][:, None, None]) & (
        row_index[None, None, :] < block_sizes[:, 1][:, None, None]
    )
    masked = jnp.where(live_mask[None], vectors, jnp.zeros((), vectors.dtype))
    first, last = masked[:, 0], masked[:, 1]

    count = lax.axis_size("bond")
    below = lax.ppermute(last, "bond", [(i, i + 1) for i in range(count - 1)])
    above = lax.ppermute(first, "bond", [(i + 1, i) for i in range(count - 1)])

    shift = term_shifts[:, None, None, None]
    zero = jnp.zeros((), vectors.dtype)
    local_first = jnp.where(shift == 0, first[None], jnp.where(shift == -1, last[None], zero))
    local_last = jnp.where(shift == 1, first[None], jnp.where(shift == 0, last[None], zero))
    local_sources = jnp.stack([local_first, local_last], axis=2)
    half_local = jnp.einsum(
        "tbik,tvbkj->tvbij", left_ops, local_sources, preferred_element_type=jnp.float32
    )
    halo = jnp.stack([below, above], axis=1)
    half_halo = jnp.einsum("tbik,vbkj->tvbij", left_ops, halo, preferred_element_type=jnp.float32)
    from_halo = jnp.stack([term_shifts == 1, term_shifts == -1], axis=1)[:, None, :, None, None]
    half = jnp.where(from_halo, half_halo, half_local).astype(jnp.bfloat16)
    partial = jnp.einsum("tvbij,tblj->vbil", half, right_ops, preferred_element_type=jnp.float32)

    op_count = lax.axis_size("op")
    share_rows = block_order // op_count
    shares = partial.astype(jnp.bfloat16).reshape(
        partial.shape[0], partial.shape[1], op_count, share_rows, block_order
    )
    received = lax.all_to_all(shares, "op", 2, 2, tiled=False)
    own_share = received.astype(jnp.float32).sum(axis=2)
    first_row = lax.axis_index("op") * share_rows
    live_share = lax.dynamic_slice_in_dim(live_mask, first_row, share_rows, 1)
    return jnp.where(live_share[None], own_share, jnp.zeros((), own_share.dtype))


def solution(mesh):
    in_specs = (
        P(None, "bond", None, None),
        P("op", "bond", None, None),
        P("op", "bond", None, None),
        P("bond", None),
        P("op"),
    )
    out_specs = P(None, "bond", "op", None)
    return jax.shard_map(
        per_device, mesh=mesh, in_specs=in_specs, out_specs=out_specs, check_vma=False
    )
```

```python
import jax
import jax.numpy as jnp
from jax import lax
from jax.sharding import PartitionSpec as P


def per_device(vectors, left_ops, right_ops, block_sizes, term_shifts):
    block_order = vectors.shape[2]
    row_index = jnp.arange(block_order, dtype=jnp.int32)
    live_mask = (row_index[None, :, None] < block_sizes[:, 0][:, None, None]) & (
        row_index[None, None, :] < block_sizes[:, 1][:, None, None]
    )
    masked = jnp.where(live_mask[None], vectors, jnp.zeros((), vectors.dtype))
    first, last = masked[:, 0], masked[:, 1]

    count = lax.axis_size("bond")
    below = lax.ppermute(last, "bond", [(i, i + 1) for i in range(count - 1)])
    above = lax.ppermute(first, "bond", [(i + 1, i) for i in range(count - 1)])

    shift = term_shifts[:, None, None, None]
    zero = jnp.zeros((), vectors.dtype)
    local_first = jnp.where(shift == 0, first[None], jnp.where(shift == -1, last[None], zero))
    local_last = jnp.where(shift == 1, first[None], jnp.where(shift == 0, last[None], zero))
    local_sources = jnp.stack([local_first, local_last], axis=2)
    half_local = jnp.einsum(
        "tbik,tvbkj->tvbij", left_ops, local_sources, preferred_element_type=jnp.float32
    ).astype(jnp.bfloat16)
    partial_local = jnp.einsum(
        "tvbij,tblj->vbil", half_local, right_ops, preferred_element_type=jnp.float32
    )
    partial_local = lax.optimization_barrier(partial_local)

    def halo_part(block, halo, uses):
        half = jnp.einsum(
            "tik,vkj->tvij", left_ops[:, block], halo, preferred_element_type=jnp.float32
        ).astype(jnp.bfloat16)
        half = jnp.where(uses[:, None, None, None], half, jnp.zeros((), half.dtype))
        return jnp.einsum("tvij,tlj->vil", half, right_ops[:, block], preferred_element_type=jnp.float32)

    partial = partial_local + jnp.stack(
        [halo_part(0, below, term_shifts == 1), halo_part(1, above, term_shifts == -1)], axis=1
    )

    op_count = lax.axis_size("op")
    share_rows = block_order // op_count
    shares = partial.astype(jnp.bfloat16).reshape(
        partial.shape[0], partial.shape[1], op_count, share_rows, block_order
    )
    received = lax.all_to_all(shares, "op", 2, 2, tiled=False)
    own_share = received.astype(jnp.float32).sum(axis=2)
    first_row = lax.axis_index("op") * share_rows
    live_share = lax.dynamic_slice_in_dim(live_mask, first_row, share_rows, 1)
    return jnp.where(live_share[None], own_share, jnp.zeros((), own_share.dtype))


def solution(mesh):
    in_specs = (
        P(None, "bond", None, None),
        P("op", "bond", None, None),
        P("op", "bond", None, None),
        P("bond", None),
        P("op"),
    )
    out_specs = P(None, "bond", "op", None)
    return jax.shard_map(
        per_device, mesh=mesh, in_specs=in_specs, out_specs=out_specs, check_vma=False
    )
```

```python
import jax
import jax.numpy as jnp
from jax import lax
from jax.sharding import PartitionSpec as P


def live_of(sizes, order):
    rows = jnp.arange(order, dtype=jnp.int32)
    return (rows[None, :, None] < sizes[:, 0][:, None, None]) & (rows[None, None, :] < sizes[:, 1][:, None, None])


def neighbours(vectors, block_sizes, order):
    count = lax.axis_size("bond")
    pad_rows = 16
    tag = jnp.zeros((vectors.shape[0], pad_rows, order), vectors.dtype)

    def packed(block):
        sizes = block_sizes[block].astype(vectors.dtype)
        return jnp.concatenate([vectors[:, block], tag.at[:, 0, 0:2].set(sizes)], axis=1)

    def unpacked(message):
        sizes = message[0, order, 0:2].astype(jnp.int32)
        live = live_of(sizes[None], order)[0]
        return jnp.where(live[None], message[:, :order], jnp.zeros((), vectors.dtype))

    below = lax.ppermute(packed(-1), "bond", [(i, i + 1) for i in range(count - 1)])
    above = lax.ppermute(packed(0), "bond", [(i + 1, i) for i in range(count - 1)])
    return unpacked(below), unpacked(above)


def per_device(vectors, left_ops, right_ops, block_sizes, term_shifts):
    block_count = vectors.shape[1]
    block_order = vectors.shape[2]
    below, above = neighbours(vectors, block_sizes, block_order)
    live_mask = live_of(block_sizes, block_order)
    masked = jnp.where(live_mask[None], vectors, jnp.zeros((), vectors.dtype))
    padded = jnp.concatenate([below[:, None], masked, above[:, None]], axis=1)

    shift = term_shifts[:, None, None, None, None]
    sources = jnp.where(
        shift == 1,
        padded[None, :, 0:block_count],
        jnp.where(shift == 0, padded[None, :, 1 : block_count + 1], padded[None, :, 2 : block_count + 2]),
    )
    half = jnp.einsum(
        "tbik,tvbkj->tvbij", left_ops, sources, preferred_element_type=jnp.float32
    ).astype(jnp.bfloat16)
    partial = jnp.einsum("tvbij,tblj->vbil", half, right_ops, preferred_element_type=jnp.float32)

    op_count = lax.axis_size("op")
    share_rows = block_order // op_count
    shares = partial.astype(jnp.bfloat16).reshape(
        partial.shape[0], block_count, op_count, share_rows, block_order
    )
    received = lax.all_to_all(shares, "op", 2, 2, tiled=False)
    own_share = received.astype(jnp.float32).sum(axis=2)
    first_row = lax.axis_index("op") * share_rows
    live_share = lax.dynamic_slice_in_dim(live_mask, first_row, share_rows, 1)
    return jnp.where(live_share[None], own_share, jnp.zeros((), own_share.dtype))


def solution(mesh):
    in_specs = (
        P(None, "bond", None, None),
        P("op", "bond", None, None),
        P("op", "bond", None, None),
        P("bond", None),
        P("op"),
    )
    out_specs = P(None, "bond", "op", None)
    return jax.shard_map(
        per_device, mesh=mesh, in_specs=in_specs, out_specs=out_specs, check_vma=False
    )
```

```python
import jax
import jax.numpy as jnp
from jax import lax
from jax.sharding import PartitionSpec as P


def extended(cells, axis, dim):
    count = lax.axis_size(axis)
    ends = count - 1
    head = lax.slice_in_dim(cells, 0, 1, axis=dim)
    tail = lax.slice_in_dim(cells, cells.shape[dim] - 1, cells.shape[dim], axis=dim)
    return jnp.concatenate(
        [
            lax.ppermute(tail, axis, [(i, (i + 1) % count) for i in range(ends)]),
            cells,
            lax.ppermute(head, axis, [((i + 1) % count, i) for i in range(ends)]),
        ],
        axis=dim,
    )


def per_device(vectors, left_ops, right_ops, block_sizes, term_shifts):
    block_count = vectors.shape[1]
    block_order = vectors.shape[2]
    row_index = jnp.arange(block_order, dtype=jnp.int32)
    live_mask = (row_index[None, :, None] < block_sizes[:, 0][:, None, None]) & (
        row_index[None, None, :] < block_sizes[:, 1][:, None, None]
    )
    masked = jnp.where(live_mask[None], vectors, jnp.zeros((), vectors.dtype))
    padded = extended(masked, "bond", 1)

    shift = term_shifts[:, None, None, None, None]
    sources = jnp.where(
        shift == 1,
        padded[None, :, 0:block_count],
        jnp.where(shift == 0, padded[None, :, 1 : block_count + 1], padded[None, :, 2 : block_count + 2]),
    )
    op_count = lax.axis_size("op")
    share_rows = block_order // op_count
    half = jnp.einsum(
        "tbik,tvbkj->tvbij", left_ops, sources, preferred_element_type=jnp.float32
    ).astype(jnp.bfloat16)
    partial = jnp.einsum("tvbij,tblj->vbil", half, right_ops, preferred_element_type=jnp.float32)

    op_count = lax.axis_size("op")
    share_rows = block_order // op_count
    shares = partial.reshape(partial.shape[0], block_count, op_count, share_rows, block_order)
    shares = shares.transpose(2, 0, 1, 3, 4).reshape(op_count, -1)
    largest = jnp.maximum(jnp.max(jnp.abs(shares), axis=1), jnp.float32(2.0**-100))
    exponent = jnp.floor(jnp.log2(largest))
    coded = (shares * jnp.exp2(14.0 - exponent)[:, None]).astype(jnp.float16)
    lane = jnp.zeros((op_count, 128), jnp.float16).at[:, 0].set(exponent.astype(jnp.float16))
    received = lax.all_to_all(jnp.concatenate([coded, lane], axis=1), "op", 0, 0, tiled=True)
    scale = jnp.exp2(received[:, -128].astype(jnp.float32) - 14.0)
    decoded = received[:, :-128].astype(jnp.float32) * scale[:, None]
    own_share = decoded.sum(axis=0).reshape(partial.shape[0], block_count, share_rows, block_order)
    first_row = lax.axis_index("op") * share_rows
    live_share = lax.dynamic_slice_in_dim(live_mask, first_row, share_rows, 1)
    return jnp.where(live_share[None], own_share, jnp.zeros((), own_share.dtype))


def solution(mesh):
    in_specs = (
        P(None, "bond", None, None),
        P("op", "bond", None, None),
        P("op", "bond", None, None),
        P("bond", None),
        P("op"),
    )
    out_specs = P(None, "bond", "op", None)
    return jax.shard_map(
        per_device, mesh=mesh, in_specs=in_specs, out_specs=out_specs, check_vma=False
    )
```

```python
import jax
import jax.numpy as jnp
from jax import lax
from jax.sharding import PartitionSpec as P


def extended(cells, axis, dim):
    count = lax.axis_size(axis)
    ends = count - 1
    head = lax.slice_in_dim(cells, 0, 1, axis=dim)
    tail = lax.slice_in_dim(cells, cells.shape[dim] - 1, cells.shape[dim], axis=dim)
    return jnp.concatenate(
        [
            lax.ppermute(tail, axis, [(i, (i + 1) % count) for i in range(ends)]),
            cells,
            lax.ppermute(head, axis, [((i + 1) % count, i) for i in range(ends)]),
        ],
        axis=dim,
    )


def per_device(vectors, left_ops, right_ops, block_sizes, term_shifts):
    block_count = vectors.shape[1]
    block_order = vectors.shape[2]
    row_index = jnp.arange(block_order, dtype=jnp.int32)
    live_mask = (row_index[None, :, None] < block_sizes[:, 0][:, None, None]) & (
        row_index[None, None, :] < block_sizes[:, 1][:, None, None]
    )
    masked = jnp.where(live_mask[None], vectors, jnp.zeros((), vectors.dtype))
    padded = extended(masked, "bond", 1)

    shift = term_shifts[:, None, None, None, None]
    sources = jnp.where(
        shift == 1,
        padded[None, :, 0:block_count],
        jnp.where(shift == 0, padded[None, :, 1 : block_count + 1], padded[None, :, 2 : block_count + 2]),
    )
    op_count = lax.axis_size("op")
    share_rows = block_order // op_count
    half = jnp.einsum(
        "tbik,tvbkj->tvbij", left_ops, sources, preferred_element_type=jnp.float32
    ).astype(jnp.bfloat16)
    partial = jnp.einsum("tvbij,tblj->vbil", half, right_ops, preferred_element_type=jnp.float32)

    op_count = lax.axis_size("op")
    share_rows = block_order // op_count
    slabs = partial.shape[0] * block_count
    shares = partial.reshape(slabs, op_count, share_rows, block_order)
    largest = jnp.maximum(jnp.max(jnp.abs(shares), axis=(0, 2, 3)), jnp.float32(2.0**-100))
    exponent = jnp.floor(jnp.log2(largest))
    coded = (shares * jnp.exp2(14.0 - exponent)[None, :, None, None]).astype(jnp.float16)
    tags = jnp.broadcast_to(exponent.astype(jnp.float16)[None, :, None, None], (1,) + shares.shape[1:])
    received = lax.all_to_all(jnp.concatenate([coded, tags], axis=0), "op", 1, 1, tiled=True)
    scale = jnp.exp2(received[slabs, :, 0, 0].astype(jnp.float32) - 14.0)
    decoded = received[:slabs].astype(jnp.float32) * scale[None, :, None, None]
    own_share = decoded.sum(axis=1).reshape(partial.shape[0], block_count, share_rows, block_order)
    first_row = lax.axis_index("op") * share_rows
    live_share = lax.dynamic_slice_in_dim(live_mask, first_row, share_rows, 1)
    return jnp.where(live_share[None], own_share, jnp.zeros((), own_share.dtype))


def solution(mesh):
    in_specs = (
        P(None, "bond", None, None),
        P("op", "bond", None, None),
        P("op", "bond", None, None),
        P("bond", None),
        P("op"),
    )
    out_specs = P(None, "bond", "op", None)
    return jax.shard_map(
        per_device, mesh=mesh, in_specs=in_specs, out_specs=out_specs, check_vma=False
    )
```

```python
import jax
import jax.numpy as jnp
from jax import lax
from jax.sharding import PartitionSpec as P


def extended(cells, axis, dim):
    count = lax.axis_size(axis)
    ends = count - 1
    head = lax.slice_in_dim(cells, 0, 1, axis=dim)
    tail = lax.slice_in_dim(cells, cells.shape[dim] - 1, cells.shape[dim], axis=dim)
    return jnp.concatenate(
        [
            lax.ppermute(tail, axis, [(i, (i + 1) % count) for i in range(ends)]),
            cells,
            lax.ppermute(head, axis, [((i + 1) % count, i) for i in range(ends)]),
        ],
        axis=dim,
    )


def per_device(vectors, left_ops, right_ops, block_sizes, term_shifts):
    block_count = vectors.shape[1]
    block_order = vectors.shape[2]
    row_index = jnp.arange(block_order, dtype=jnp.int32)
    live_mask = (row_index[None, :, None] < block_sizes[:, 0][:, None, None]) & (
        row_index[None, None, :] < block_sizes[:, 1][:, None, None]
    )
    masked = jnp.where(live_mask[None], vectors, jnp.zeros((), vectors.dtype))
    padded = extended(masked, "bond", 1)

    shift = term_shifts[:, None, None, None, None]
    sources = jnp.where(
        shift == 1,
        padded[None, :, 0:block_count],
        jnp.where(shift == 0, padded[None, :, 1 : block_count + 1], padded[None, :, 2 : block_count + 2]),
    )
    op_count = lax.axis_size("op")
    share_rows = block_order // op_count
    half = jnp.einsum(
        "tbik,tvbkj->tvbij", left_ops, sources, preferred_element_type=jnp.float32
    ).astype(jnp.bfloat16)
    partial = jnp.einsum("tvbij,tblj->vbil", half, right_ops, preferred_element_type=jnp.float32)

    op_count = lax.axis_size("op")
    share_rows = block_order // op_count
    source_max = jnp.max(jnp.abs(padded.astype(jnp.float32)))
    bound = 65536.0 * 1.01 * source_max * left_ops.shape[0] * 0.03125 * 0.375
    exponent = jnp.ceil(jnp.log2(jnp.maximum(bound, jnp.float32(2.0**-100))))
    shares = (partial * jnp.exp2(14.0 - exponent)).astype(jnp.float16).reshape(
        partial.shape[0], block_count, op_count, share_rows, block_order
    )
    received = lax.all_to_all(shares, "op", 2, 2, tiled=False)
    own_share = received.astype(jnp.float32).sum(axis=2) * jnp.exp2(exponent - 14.0)
    first_row = lax.axis_index("op") * share_rows
    live_share = lax.dynamic_slice_in_dim(live_mask, first_row, share_rows, 1)
    return jnp.where(live_share[None], own_share, jnp.zeros((), own_share.dtype))


def solution(mesh):
    in_specs = (
        P(None, "bond", None, None),
        P("op", "bond", None, None),
        P("op", "bond", None, None),
        P("bond", None),
        P("op"),
    )
    out_specs = P(None, "bond", "op", None)
    return jax.shard_map(
        per_device, mesh=mesh, in_specs=in_specs, out_specs=out_specs, check_vma=False
    )
```

```python
import jax
import jax.numpy as jnp
from jax import lax
from jax.sharding import PartitionSpec as P


def per_device(vectors, left_ops, right_ops, block_sizes, term_shifts):
    block_count = vectors.shape[1]
    block_order = vectors.shape[2]
    row_index = jnp.arange(block_order, dtype=jnp.int32)
    live_mask = (row_index[None, :, None] < block_sizes[:, 0][:, None, None]) & (
        row_index[None, None, :] < block_sizes[:, 1][:, None, None]
    )
    masked = jnp.where(live_mask[None], vectors, jnp.zeros((), vectors.dtype))
    count = lax.axis_size("bond")
    first, last = masked[:, 0], masked[:, 1]
    below = lax.ppermute(last, "bond", [(i, i + 1) for i in range(count - 1)])
    above = lax.ppermute(first, "bond", [(i + 1, i) for i in range(count - 1)])

    shift = term_shifts[:, None, None, None]
    source_first = jnp.where(shift == 1, below[None], jnp.where(shift == 0, first[None], last[None]))
    source_last = jnp.where(shift == 1, first[None], jnp.where(shift == 0, last[None], above[None]))
    sources = jnp.stack([source_first, source_last], axis=2)
    op_count = lax.axis_size("op")
    share_rows = block_order // op_count
    half = jnp.einsum(
        "tbik,tvbkj->tvbij", left_ops, sources, preferred_element_type=jnp.float32
    ).astype(jnp.bfloat16)
    partial = jnp.einsum("tvbij,tblj->vbil", half, right_ops, preferred_element_type=jnp.float32)

    op_count = lax.axis_size("op")
    share_rows = block_order // op_count
    source_max = jnp.maximum(
        jnp.max(jnp.abs(masked.astype(jnp.float32))),
        jnp.maximum(jnp.max(jnp.abs(below.astype(jnp.float32))), jnp.max(jnp.abs(above.astype(jnp.float32)))),
    )
    bound = 65536.0 * 1.01 * source_max * left_ops.shape[0] * 0.03125 * 0.375
    exponent = jnp.ceil(jnp.log2(jnp.maximum(bound, jnp.float32(2.0**-100))))
    shares = (partial * jnp.exp2(14.0 - exponent)).astype(jnp.float16).reshape(
        partial.shape[0], block_count, op_count, share_rows, block_order
    )
    received = lax.all_to_all(shares, "op", 2, 2, tiled=False)
    own_share = received.astype(jnp.float32).sum(axis=2) * jnp.exp2(exponent - 14.0)
    first_row = lax.axis_index("op") * share_rows
    live_share = lax.dynamic_slice_in_dim(live_mask, first_row, share_rows, 1)
    return jnp.where(live_share[None], own_share, jnp.zeros((), own_share.dtype))


def solution(mesh):
    in_specs = (
        P(None, "bond", None, None),
        P("op", "bond", None, None),
        P("op", "bond", None, None),
        P("bond", None),
        P("op"),
    )
    out_specs = P(None, "bond", "op", None)
    return jax.shard_map(
        per_device, mesh=mesh, in_specs=in_specs, out_specs=out_specs, check_vma=False
    )
```
